32 devices in a mesh: expert: 8 (over z, x), tensor: 4 (over y, core).
Axes of the slice: x: 2, y: 2, z: 4, core: 2. Of those that a mesh axis runs over, the one named last changes fastest.
Arguments:
- attn_heads: bfloat16 [1024, 4096], P('expert', 'tensor'), may hold values from -6 to 6
- out_proj: bfloat16 [4096, 4096], P('tensor', 'expert'), may hold values from -0.09375 to 0.09375
- residual: bfloat16 [1024, 4096], P('expert'), may hold values from -6 to 6
- norm_gain: bfloat16 [4096], replicated, may hold values from 0.099609375 to 1.8984375
- gate_proj: bfloat16 [16, 1536, 4096], P('expert', 'tensor'), may hold values from -0.09375 to 0.09375
- up_proj: bfloat16 [16, 1536, 4096], P('expert', 'tensor'), may hold values from -0.09375 to 0.09375
- down_proj: bfloat16 [16, 1536, 4096], P('expert', None, 'tensor'), may hold values from -0.15625 to 0.15625
- expert_ids: int32 [1024, 8], P('expert'), may hold values from 0 to 15, all different within a row; in each aligned block of 128 rows (0 to 127, 128 to 255, ...) at most 96 rows name the same one
- gate_scores: float32 [1024, 8], P('expert'), may hold values from 0.25 to 1
Outputs:
- layer_out: bfloat16 [1024, 4096], P('expert', 'tensor')
The draws below stay inside these ranges and needn't reach their ends.
Inputs may be any that keep to these rules, and one draw needn't show every extreme that they name: `expert_ids`: each row names 8 different experts. Among the 128 rows of one device no expert is named by more than 96 rows, a bound that some block reaches.
All inputs are finite; a program needn't handle non-finite values.
Results may differ from the reference program's by a relative error of at most 0.0051.
Values may be sent and summed in bfloat16 or wider, within the bound.
No kernel may reach another device: no remote copies, remote signals or barrier semaphores. Data moves between devices by JAX's collectives and lax.ppermute only.
A program may use at most 128 MiB of HBM per device.

```python
import math
import jax
import jax.numpy as jnp
import numpy as np
from jax import lax

D = 4096
FF = 1536
HEADS = 32
HD = 128
TOP = 8
TOK_DEV = 128
EXPERTS = 16
CAP = 96
TOKENS = 1024
N_EXPERT = 8


def block_scale(own_key, shape, cuts, smallest, high):
    def one(position, shards_of):
        heights = jax.random.uniform(jax.random.fold_in(jax.random.fold_in(own_key, 6), position), (shards_of,), jnp.float32, smallest / len(cuts), high / len(cuts))
        return jnp.repeat(jnp.exp(heights), shape[position] // shards_of).reshape((-1,) + (1,) * (len(shape) - position - 1))

    factor_of = one(*cuts[0])
    for cut in cuts[1:]:
        factor_of = factor_of * one(*cut)
    return factor_of


def assign_block(rng, own, number, rows, number_of, top, limit, lean):
    ranking = jax.random.permutation(rng, number_of)
    crowded, ordinary = shares(number_of, rows * top, limit, lean, True), shares(number_of, rows * top, limit, lean, False)
    places = jnp.arange(number_of)

    def named(sizes, turn):
        used = int((sizes > 0).sum())
        fixed = max(1, used // 4)
        shifted = fixed + (places - fixed + turn * (used - fixed)) % max(1, number_of - fixed)
        return jnp.zeros((number_of,), jnp.int32).at[ranking[jnp.where(places < fixed, places, shifted)]].set(jnp.asarray(sizes, jnp.int32))

    sizes = jnp.where(number % 4 == 0, named(crowded, number // 4), named(ordinary, number - number // 4 - 1))
    mixed = jax.random.permutation(jax.random.fold_in(own, 3), number_of)
    source_of, taker = mixed[0:number_of // 2 * 2:2], mixed[1:number_of // 2 * 2:2]
    slack = jnp.minimum(sizes[source_of] - 1, limit - sizes[taker]) // 2
    slack = jnp.where((source_of == ranking[0]) | (taker == ranking[0]) | (sizes[taker] == 0), 0, jnp.maximum(slack, 0))
    shifted = jax.random.randint(jax.random.fold_in(own, 4), (number_of // 2,), 0, 1 << 20) % (slack + 1)
    sizes = sizes.at[source_of].add(-shifted).at[taker].add(shifted)
    members = jnp.searchsorted(jnp.cumsum(sizes), jnp.arange(rows * top), side="right").astype(jnp.int32)
    listing = members.reshape(top, rows).T
    listing = listing[jax.random.permutation(jax.random.fold_in(own, 1), rows)]
    turn = jax.random.randint(jax.random.fold_in(own, 2), (rows, 1), 0, top)
    return jnp.take_along_axis(listing, (jnp.arange(top)[None, :] + turn) % top, axis=1)


def shares(number_of, total, bound, skew, full):
    loads = [(1 << 20) // math.isqrt(standing ** skew) + 1 for standing in range(1, number_of + 1)]
    largest = bound if full else min(bound, max(-(-total // number_of), total * loads[0] // sum(loads)))
    least = 1 if total - largest >= number_of - 1 else 0
    holding, rest = [largest] + [least] * (number_of - 1), total - largest - least * (number_of - 1)
    while rest > 0:
        movable = [i for i in range(1, number_of) if holding[i] < largest] or [i for i in range(1, number_of) if holding[i] < bound]
        whole, left = sum([loads[i] for i in movable]), rest
        for i in movable:
            addition = min(bound - holding[i], max(1, left * loads[i] // whole), rest)
            holding[i] = holding[i] + addition
            rest = rest - addition
    return np.array(holding)


def gaussian(key, dims, deviation, most, cuts=(), kind=jnp.bfloat16):
    gain = block_scale(key, dims, cuts, -0.22, 0.18) if cuts else 1.0
    values = jax.random.normal(key, dims, jnp.float32) * deviation * gain
    return jnp.minimum(jnp.maximum(values, -most), most).astype(kind)


def setup_inputs(seed: int = 0) -> dict:
    key_list = jax.random.split(jax.random.key(seed), 10)
    attn_heads = gaussian(key_list[0], (TOKENS, HEADS * HD), 1.0, 6.0, ((0, 8), (1, 4)))
    out_proj = gaussian(key_list[1], (HEADS * HD, D), (HEADS * HD) ** -0.5, 0.09375, ((0, 4), (1, 8)))
    residual = gaussian(key_list[2], (TOKENS, D), 1.0, 6.0, ((0, 8),))
    norm_gain = jnp.clip(1.0 + 0.18 * jax.random.normal(key_list[3], (D,), jnp.float32), 0.099609375, 1.8984375).astype(jnp.bfloat16)
    gate_proj = gaussian(key_list[4], (EXPERTS, FF, D), D ** -0.5, 0.09375, ((0, 8), (1, 4)))
    up_proj = gaussian(key_list[5], (EXPERTS, FF, D), D ** -0.5, 0.09375, ((0, 8), (1, 4)))
    down_proj = gaussian(key_list[6], (EXPERTS, FF, D), FF ** -0.5, 0.15625, ((0, 8), (2, 4)))
    expert_ids_keys = jax.random.split(jax.random.fold_in(key_list[7], 1), TOKENS // TOK_DEV)
    expert_ids_turns = jax.random.permutation(jax.random.fold_in(key_list[7], 3), TOKENS // TOK_DEV)
    expert_ids = jax.vmap(lambda own, number: assign_block(jax.random.fold_in(key_list[7], 2), own, number, TOK_DEV, EXPERTS, TOP, CAP, 2))(expert_ids_keys, expert_ids_turns).reshape((TOKENS, TOP))
    gate_scores = jnp.clip(jnp.exp(math.log(1.0) - 1.3862944 * jax.random.uniform(key_list[8], (TOKENS, TOP), jnp.float32) ** block_scale(key_list[8], (TOKENS, TOP), ((0, 8),), -0.2, 0.2)), 0.25, 1.0)
    return dict(attn_heads=attn_heads, out_proj=out_proj, residual=residual, norm_gain=norm_gain, gate_proj=gate_proj, up_proj=up_proj, down_proj=down_proj, expert_ids=expert_ids, gate_scores=gate_scores)


EPS = 1e-06

def route(ids):
    picks = ids[:, :, None] == jnp.arange(EXPERTS, dtype=jnp.int32)[None, None, :]
    flag = lax.optimization_barrier(jnp.sum(picks.astype(jnp.int32), axis=1))
    before = jnp.cumsum(flag, axis=0) - flag
    rank = lax.optimization_barrier(jnp.sum(jnp.where(picks, before[:, None, :], 0), axis=2))
    return (ids * CAP + rank).astype(jnp.int32)

def reference(attn_heads, out_proj, residual, norm_gain, gate_proj, up_proj, down_proj, expert_ids, gate_scores):
    attn = jnp.dot(attn_heads, out_proj, preferred_element_type=jnp.float32)
    state = (residual.astype(jnp.float32) + attn).astype(jnp.bfloat16)
    state_f = state.astype(jnp.float32)
    var = lax.optimization_barrier(jnp.mean(state_f * state_f, axis=1, keepdims=True))
    normed = (state_f * lax.rsqrt(var + EPS) * norm_gain.astype(jnp.float32)).astype(jnp.bfloat16)
    weights = gate_scores / lax.optimization_barrier(jnp.sum(gate_scores, axis=1, keepdims=True))
    ids = expert_ids.reshape(N_EXPERT, TOK_DEV, TOP)
    slots = jax.vmap(route)(ids)
    token = jnp.broadcast_to(jnp.arange(TOKENS, dtype=jnp.int32).reshape(N_EXPERT, TOK_DEV, 1), (N_EXPERT, TOK_DEV, TOP))
    owner = jax.vmap(lambda s, t: jnp.zeros((EXPERTS * CAP,), jnp.int32).at[s.reshape(-1)].set(t.reshape(-1) + 1))(slots, token)
    wtab = jax.vmap(lambda s, w: jnp.zeros((EXPERTS * CAP,), jnp.float32).at[s.reshape(-1)].set(w.reshape(-1)))(slots, weights.reshape(N_EXPERT, TOK_DEV, TOP))
    owner = owner.reshape(N_EXPERT, EXPERTS, CAP).transpose(1, 0, 2).reshape(EXPERTS, N_EXPERT * CAP)
    wtab = wtab.reshape(N_EXPERT, EXPERTS, CAP).transpose(1, 0, 2).reshape(EXPERTS, N_EXPERT * CAP)

    def step(total, item):
        idx, wts, gmat, umat, dmat = item
        place = jnp.maximum(idx - 1, 0).astype(jnp.int32)
        rows = jnp.where((idx > 0)[:, None], normed[place], jnp.zeros((), jnp.bfloat16)).astype(jnp.float32)
        gate = jnp.dot(rows, gmat.astype(jnp.float32).T)
        upper = jnp.dot(rows, umat.astype(jnp.float32).T)
        act = (jax.nn.silu(gate) * upper).astype(jnp.bfloat16)
        out = jnp.dot(act.astype(jnp.float32), dmat.astype(jnp.float32)).astype(jnp.bfloat16)
        total = total.at[place].add(wts[:, None] * out.astype(jnp.float32))
        return (total, None)
    total, _ = lax.scan(step, jnp.zeros((TOKENS, D), jnp.float32), (owner, wtab, gate_proj, up_proj, down_proj))
    return (state_f + total).astype(jnp.bfloat16)
```

```python
import jax
import jax.numpy as jnp
from jax import lax
from jax.sharding import PartitionSpec as P

EPS = 1e-06


def on_device(
    attn_heads,
    out_proj,
    residual,
    norm_gain,
    gate_proj,
    up_proj,
    down_proj,
    expert_ids,
    gate_scores,
):
    tok_count = residual.shape[0]
    width = residual.shape[1]
    groups = lax.axis_size("expert")
    tensor_ways = lax.axis_size("tensor")
    exp_local = gate_proj.shape[0]
    hidden_local = gate_proj.shape[1]
    share = width // tensor_ways
    cols_e = out_proj.shape[1]
    cols_et = cols_e // tensor_ways
    me_e = lax.axis_index("expert")
    me_t = lax.axis_index("tensor")
    all_tok = groups * tok_count

    heads_all = lax.all_gather(attn_heads, "expert", axis=0, tiled=True)
    partial = jnp.dot(heads_all, out_proj, preferred_element_type=jnp.float32)
    summed = lax.psum_scatter(partial, "tensor", scatter_dimension=1, tiled=True)
    mine = lax.all_to_all(
        summed.reshape(groups, tok_count, cols_et), "expert", 0, 0, tiled=False
    )
    res_cols = lax.dynamic_index_in_dim(
        residual.reshape(tok_count, groups, tensor_ways, cols_et), me_t, 2, keepdims=False
    )
    state_ct = (jnp.transpose(res_cols, (1, 0, 2)).astype(jnp.float32) + mine).astype(
        jnp.bfloat16
    )
    state_all = lax.all_gather(state_ct, "tensor", axis=0, tiled=False)
    state = jnp.transpose(state_all, (2, 1, 0, 3)).reshape(tok_count, width)
    state_f = state.astype(jnp.float32)

    squares = jnp.sum(state_f * state_f, axis=1, keepdims=True)
    scale = lax.rsqrt(squares / width + EPS)
    state_q = lax.dynamic_slice_in_dim(state_f, me_t * share, share, 1)
    gain_q = lax.dynamic_slice_in_dim(norm_gain, me_t * share, share, 0).astype(jnp.float32)
    normed_q = (state_q * scale * gain_q).astype(jnp.bfloat16)

    rows_q = lax.all_gather(normed_q, "expert", axis=0, tiled=True)
    rows = lax.all_gather(rows_q, "tensor", axis=0, tiled=False)

    ids_all = lax.all_gather(expert_ids, "expert", axis=0, tiled=True)
    scores_all = lax.all_gather(gate_scores, "expert", axis=0, tiled=True)
    weights = scores_all / jnp.sum(scores_all, axis=1, keepdims=True)

    total = jnp.zeros((all_tok, share), jnp.float32)
    for loc in range(exp_local):
        glob = me_e * exp_local + loc
        hit = ids_all == glob
        w_tok = jnp.sum(jnp.where(hit, weights, 0.0), axis=1)
        chosen = jnp.any(hit, axis=1)
        gmat = gate_proj[loc].reshape(hidden_local, tensor_ways, share)
        umat = up_proj[loc].reshape(hidden_local, tensor_ways, share)
        gate = jnp.einsum("ard,fad->rf", rows, gmat, preferred_element_type=jnp.float32)
        upper = jnp.einsum("ard,fad->rf", rows, umat, preferred_element_type=jnp.float32)
        act = (jax.nn.silu(gate) * upper).astype(jnp.bfloat16)
        act_all = lax.all_gather(act, "tensor", axis=0, tiled=False)
        dmat = down_proj[loc].reshape(tensor_ways, hidden_local, share)
        out = jnp.einsum(
            "arf,afd->rd", act_all, dmat, preferred_element_type=jnp.float32
        ).astype(jnp.bfloat16)
        total = total + jnp.where(
            chosen[:, None], w_tok[:, None] * out.astype(jnp.float32), 0.0
        )
    mixture = lax.psum_scatter(total, "expert", scatter_dimension=0, tiled=True)
    state_out = lax.dynamic_slice_in_dim(state_f, me_t * share, share, 1)
    return (state_out + mixture).astype(jnp.bfloat16)


def solution(mesh):
    in_specs = (
        P("expert", "tensor"),
        P("tensor", "expert"),
        P("expert", None),
        P(),
        P("expert", "tensor", None),
        P("expert", "tensor", None),
        P("expert", None, "tensor"),
        P("expert", None),
        P("expert", None),
    )
    out_specs = P("expert", "tensor")
    return jax.shard_map(
        on_device, mesh=mesh, in_specs=in_specs, out_specs=out_specs, check_vma=False
    )
```

```python
import jax
import jax.numpy as jnp
from jax import lax
from jax.sharding import PartitionSpec as P

EPS = 1e-06
CHUNKS = 2


def on_device(
    attn_heads,
    out_proj,
    residual,
    norm_gain,
    gate_proj,
    up_proj,
    down_proj,
    expert_ids,
    gate_scores,
):
    tok_count = residual.shape[0]
    width = residual.shape[1]
    groups = lax.axis_size("expert")
    tensor_ways = lax.axis_size("tensor")
    exp_local = gate_proj.shape[0]
    hidden_local = gate_proj.shape[1]
    share = width // tensor_ways
    cols_e = out_proj.shape[1]
    cols_et = cols_e // tensor_ways
    me_e = lax.axis_index("expert")
    me_t = lax.axis_index("tensor")
    all_tok = groups * tok_count

    heads_all = lax.all_gather(attn_heads, "expert", axis=0, tiled=True)
    partial = jnp.dot(heads_all, out_proj, preferred_element_type=jnp.float32)
    summed = lax.psum_scatter(partial, "tensor", scatter_dimension=1, tiled=True)
    mine = lax.all_to_all(
        summed.reshape(groups, tok_count, cols_et), "expert", 0, 0, tiled=False
    )
    res_cols = lax.dynamic_index_in_dim(
        residual.reshape(tok_count, groups, tensor_ways, cols_et), me_t, 2, keepdims=False
    )
    state_ct = (jnp.transpose(res_cols, (1, 0, 2)).astype(jnp.float32) + mine).astype(
        jnp.bfloat16
    )
    state_all = lax.all_gather(state_ct, "tensor", axis=0, tiled=False)
    state = jnp.transpose(state_all, (2, 1, 0, 3)).reshape(tok_count, width)
    state_f = state.astype(jnp.float32)

    squares = jnp.sum(state_f * state_f, axis=1, keepdims=True)
    scale = lax.rsqrt(squares / width + EPS)
    state_q = lax.dynamic_slice_in_dim(state_f, me_t * share, share, 1)
    gain_q = lax.dynamic_slice_in_dim(norm_gain, me_t * share, share, 0).astype(jnp.float32)
    normed_q = (state_q * scale * gain_q).astype(jnp.bfloat16)

    experts_all = groups * exp_local
    hit_src = expert_ids[:, :, None] == jnp.arange(experts_all, dtype=jnp.int32)[None, None, :]
    weights = gate_scores / jnp.sum(gate_scores, axis=1, keepdims=True)
    w_src = jnp.sum(jnp.where(hit_src, weights[:, :, None], 0.0), axis=1)
    w_all = lax.all_gather(w_src.reshape(-1), "expert", axis=0, tiled=True).reshape(
        all_tok, experts_all
    )
    w_mine = lax.dynamic_slice_in_dim(w_all, me_e * exp_local, exp_local, 1)

    rows_q = lax.all_gather(normed_q, "expert", axis=0, tiled=True)
    rows = lax.all_gather(rows_q, "tensor", axis=1, tiled=True)

    chunk = tok_count // CHUNKS
    rows_c = rows.reshape(groups, CHUNKS, chunk, width)
    w_c = w_mine.reshape(groups, CHUNKS, chunk, exp_local)
    pieces = []
    for c in range(CHUNKS):
        x = rows_c[:, c].reshape(groups * chunk, width)
        wc = w_c[:, c].reshape(groups * chunk, exp_local)
        total = jnp.zeros((groups * chunk, share), jnp.float32)
        for loc in range(exp_local):
            gate = jnp.dot(x, gate_proj[loc].T, preferred_element_type=jnp.float32)
            upper = jnp.dot(x, up_proj[loc].T, preferred_element_type=jnp.float32)
            act = (jax.nn.silu(gate) * upper).astype(jnp.bfloat16)
            act_all = lax.all_gather(act, "tensor", axis=1, tiled=True)
            out = jnp.dot(
                act_all, down_proj[loc], preferred_element_type=jnp.float32
            ).astype(jnp.bfloat16)
            w_tok = wc[:, loc][:, None]
            total = total + jnp.where(w_tok > 0, w_tok * out.astype(jnp.float32), 0.0)
        pieces.append(lax.psum_scatter(total, "expert", scatter_dimension=0, tiled=True))
    mixture = jnp.concatenate(pieces, axis=0)
    state_out = lax.dynamic_slice_in_dim(state_f, me_t * share, share, 1)
    return (state_out + mixture).astype(jnp.bfloat16)


def solution(mesh):
    in_specs = (
        P("expert", "tensor"),
        P("tensor", "expert"),
        P("expert", None),
        P(),
        P("expert", "tensor", None),
        P("expert", "tensor", None),
        P("expert", None, "tensor"),
        P("expert", None),
        P("expert", None),
    )
    out_specs = P("expert", "tensor")
    return jax.shard_map(
        on_device, mesh=mesh, in_specs=in_specs, out_specs=out_specs, check_vma=False
    )
```

```python
import jax
import jax.numpy as jnp
from jax import lax
from jax.sharding import PartitionSpec as P

EPS = 1e-06
CHUNKS = 1


def on_device(
    attn_heads,
    out_proj,
    residual,
    norm_gain,
    gate_proj,
    up_proj,
    down_proj,
    expert_ids,
    gate_scores,
):
    tok_count = residual.shape[0]
    width = residual.shape[1]
    groups = lax.axis_size("expert")
    tensor_ways = lax.axis_size("tensor")
    exp_local = gate_proj.shape[0]
    hidden_local = gate_proj.shape[1]
    share = width // tensor_ways
    cols_e = out_proj.shape[1]
    cols_et = cols_e // tensor_ways
    me_e = lax.axis_index("expert")
    me_t = lax.axis_index("tensor")
    all_tok = groups * tok_count

    heads_all = lax.all_gather(attn_heads, "expert", axis=0, tiled=True)
    partial = jnp.dot(heads_all, out_proj, preferred_element_type=jnp.float32)
    summed = lax.psum_scatter(partial, "tensor", scatter_dimension=1, tiled=True)
    mine = lax.all_to_all(
        summed.reshape(groups, tok_count, cols_et), "expert", 0, 0, tiled=False
    )
    res_cols = lax.dynamic_index_in_dim(
        residual.reshape(tok_count, groups, tensor_ways, cols_et), me_t, 2, keepdims=False
    )
    state_ct = (jnp.transpose(res_cols, (1, 0, 2)).astype(jnp.float32) + mine).astype(
        jnp.bfloat16
    )
    state_all = lax.all_gather(state_ct, "tensor", axis=0, tiled=False)
    state = jnp.transpose(state_all, (2, 1, 0, 3)).reshape(tok_count, width)
    state_f = state.astype(jnp.float32)

    squares = jnp.sum(state_f * state_f, axis=1, keepdims=True)
    scale = lax.rsqrt(squares / width + EPS)
    state_q = lax.dynamic_slice_in_dim(state_f, me_t * share, share, 1)
    gain_q = lax.dynamic_slice_in_dim(norm_gain, me_t * share, share, 0).astype(jnp.float32)
    normed_q = (state_q * scale * gain_q).astype(jnp.bfloat16)

    experts_all = groups * exp_local
    hit_src = expert_ids[:, :, None] == jnp.arange(experts_all, dtype=jnp.int32)[None, None, :]
    weights = gate_scores / jnp.sum(gate_scores, axis=1, keepdims=True)
    w_src = jnp.sum(jnp.where(hit_src, weights[:, :, None], 0.0), axis=1)
    hi = w_src.astype(jnp.bfloat16)
    rest = w_src - hi.astype(jnp.float32)
    mid = rest.astype(jnp.bfloat16)
    lo = (rest - mid.astype(jnp.float32)).astype(jnp.bfloat16)
    coded = jnp.stack([hi, mid, lo]).reshape(-1)
    extra = -(-coded.shape[0] // (share * 8)) * 8
    coded = jnp.pad(coded, (0, extra * share - coded.shape[0])).reshape(extra, share)
    packet = jnp.concatenate([normed_q, coded], axis=0)

    got = lax.all_gather(packet, ("expert", "tensor"), axis=0, tiled=False).reshape(
        groups, tensor_ways, tok_count + extra, share
    )
    rows = jnp.transpose(got[:, :, :tok_count], (0, 2, 1, 3)).reshape(all_tok, width)
    parts = got[:, 0, tok_count:].reshape(groups, -1)[:, : 3 * tok_count * experts_all]
    parts = parts.reshape(groups, 3, tok_count, experts_all).astype(jnp.float32)
    w_all = (parts[:, 0] + parts[:, 1] + parts[:, 2]).reshape(all_tok, experts_all)
    w_mine = lax.dynamic_slice_in_dim(w_all, me_e * exp_local, exp_local, 1)

    chunk = tok_count // CHUNKS
    rows_c = rows.reshape(groups, CHUNKS, chunk, width)
    w_c = w_mine.reshape(groups, CHUNKS, chunk, exp_local)
    pieces = []
    for c in range(CHUNKS):
        x = rows_c[:, c].reshape(groups * chunk, width)
        wc = w_c[:, c].reshape(groups * chunk, exp_local)
        total = jnp.zeros((groups * chunk, share), jnp.float32)
        for loc in range(exp_local):
            gate = jnp.dot(x, gate_proj[loc].T, preferred_element_type=jnp.float32)
            upper = jnp.dot(x, up_proj[loc].T, preferred_element_type=jnp.float32)
            act = (jax.nn.silu(gate) * upper).astype(jnp.bfloat16)
            act_all = lax.all_gather(act, "tensor", axis=1, tiled=True)
            out = jnp.dot(
                act_all, down_proj[loc], preferred_element_type=jnp.float32
            ).astype(jnp.bfloat16)
            w_tok = wc[:, loc][:, None]
            total = total + jnp.where(w_tok > 0, w_tok * out.astype(jnp.float32), 0.0)
        pieces.append(lax.psum_scatter(total, "expert", scatter_dimension=0, tiled=True))
    mixture = jnp.concatenate(pieces, axis=0)
    state_out = lax.dynamic_slice_in_dim(state_f, me_t * share, share, 1)
    return (state_out + mixture).astype(jnp.bfloat16)


def solution(mesh):
    in_specs = (
        P("expert", "tensor"),
        P("tensor", "expert"),
        P("expert", None),
        P(),
        P("expert", "tensor", None),
        P("expert", "tensor", None),
        P("expert", None, "tensor"),
        P("expert", None),
        P("expert", None),
    )
    out_specs = P("expert", "tensor")
    return jax.shard_map(
        on_device, mesh=mesh, in_specs=in_specs, out_specs=out_specs, check_vma=False
    )
```

```python
import jax
import jax.numpy as jnp
from jax import lax
from jax.sharding import PartitionSpec as P

EPS = 1e-06


def on_device(
    attn_heads,
    out_proj,
    residual,
    norm_gain,
    gate_proj,
    up_proj,
    down_proj,
    expert_ids,
    gate_scores,
):
    tok_count = residual.shape[0]
    width = residual.shape[1]
    groups = lax.axis_size("expert")
    tensor_ways = lax.axis_size("tensor")
    exp_local = gate_proj.shape[0]
    hidden_local = gate_proj.shape[1]
    share = width // tensor_ways
    cols_e = out_proj.shape[1]
    cols_et = cols_e // tensor_ways
    me_e = lax.axis_index("expert")
    me_t = lax.axis_index("tensor")
    all_tok = groups * tok_count

    experts_all = groups * exp_local
    hit_src = expert_ids[:, :, None] == jnp.arange(experts_all, dtype=jnp.int32)[None, None, :]
    weights = gate_scores / jnp.sum(gate_scores, axis=1, keepdims=True)
    w_src = jnp.sum(jnp.where(hit_src, weights[:, :, None], 0.0), axis=1)
    hi = w_src.astype(jnp.bfloat16)
    rest = w_src - hi.astype(jnp.float32)
    mid = rest.astype(jnp.bfloat16)
    lo = (rest - mid.astype(jnp.float32)).astype(jnp.bfloat16)
    coded = jnp.stack([hi, mid, lo]).reshape(-1)
    heads_w = attn_heads.shape[1]
    extra = -(-coded.shape[0] // (heads_w * 8)) * 8
    coded = jnp.pad(coded, (0, extra * heads_w - coded.shape[0])).reshape(extra, heads_w)
    packet = jnp.concatenate([attn_heads, coded], axis=0)

    got = lax.all_gather(packet, "expert", axis=0, tiled=False)
    partial = jnp.einsum(
        "enh,hc->enc", got[:, :tok_count], out_proj, preferred_element_type=jnp.float32
    ).reshape(all_tok, cols_e)
    parts = got[:, tok_count:].reshape(groups, -1)[:, : 3 * tok_count * experts_all]
    parts = parts.reshape(groups, 3, tok_count, experts_all).astype(jnp.float32)
    w_all = (parts[:, 0] + parts[:, 1] + parts[:, 2]).reshape(all_tok, experts_all)
    w_mine = lax.dynamic_slice_in_dim(w_all, me_e * exp_local, exp_local, 1)
    summed = lax.psum_scatter(partial, "tensor", scatter_dimension=1, tiled=True)
    mine = lax.all_to_all(
        summed.reshape(groups, tok_count, cols_et), "expert", 0, 0, tiled=False
    )
    res_cols = lax.dynamic_index_in_dim(
        residual.reshape(tok_count, groups, tensor_ways, cols_et), me_t, 2, keepdims=False
    )
    state_ct = (jnp.transpose(res_cols, (1, 0, 2)).astype(jnp.float32) + mine).astype(
        jnp.bfloat16
    )
    state_all = lax.all_gather(state_ct, "tensor", axis=0, tiled=False)
    state = jnp.transpose(state_all, (2, 1, 0, 3)).reshape(tok_count, width)
    state_f = state.astype(jnp.float32)

    squares = jnp.sum(state_f * state_f, axis=1, keepdims=True)
    scale = lax.rsqrt(squares / width + EPS)
    state_q = lax.dynamic_slice_in_dim(state_f, me_t * share, share, 1)
    gain_q = lax.dynamic_slice_in_dim(norm_gain, me_t * share, share, 0).astype(jnp.float32)
    normed_q = (state_q * scale * gain_q).astype(jnp.bfloat16)

    slabs = lax.all_gather(normed_q, ("tensor", "expert"), axis=0, tiled=False).reshape(
        tensor_ways, all_tok, share
    )

    total = jnp.zeros((all_tok, share), jnp.float32)
    for loc in range(exp_local):
        gate = None
        upper = None
        for a in range(tensor_ways):
            x = slabs[a]
            gpart = jnp.dot(
                x, gate_proj[loc, :, a * share : (a + 1) * share].T,
                preferred_element_type=jnp.float32,
            )
            upart = jnp.dot(
                x, up_proj[loc, :, a * share : (a + 1) * share].T,
                preferred_element_type=jnp.float32,
            )
            gate = gpart if gate is None else gate + gpart
            upper = upart if upper is None else upper + upart
        act = (jax.nn.silu(gate) * upper).astype(jnp.bfloat16)
        act_all = lax.all_gather(act, "tensor", axis=1, tiled=True)
        out = jnp.dot(
            act_all, down_proj[loc], preferred_element_type=jnp.float32
        ).astype(jnp.bfloat16)
        w_tok = w_mine[:, loc][:, None]
        total = total + jnp.where(w_tok > 0, w_tok * out.astype(jnp.float32), 0.0)
    mixture = lax.psum_scatter(total, "expert", scatter_dimension=0, tiled=True)
    state_out = lax.dynamic_slice_in_dim(state_f, me_t * share, share, 1)
    return (state_out + mixture).astype(jnp.bfloat16)


def solution(mesh):
    in_specs = (
        P("expert", "tensor"),
        P("tensor", "expert"),
        P("expert", None),
        P(),
        P("expert", "tensor", None),
        P("expert", "tensor", None),
        P("expert", None, "tensor"),
        P("expert", None),
        P("expert", None),
    )
    out_specs = P("expert", "tensor")
    return jax.shard_map(
        on_device, mesh=mesh, in_specs=in_specs, out_specs=out_specs, check_vma=False
    )
```

```python
import jax
import jax.numpy as jnp
from jax import lax
from jax.sharding import PartitionSpec as P

EPS = 1e-06


def on_device(
    attn_heads,
    out_proj,
    residual,
    norm_gain,
    gate_proj,
    up_proj,
    down_proj,
    expert_ids,
    gate_scores,
):
    tok_count = residual.shape[0]
    width = residual.shape[1]
    groups = lax.axis_size("expert")
    tensor_ways = lax.axis_size("tensor")
    exp_local = gate_proj.shape[0]
    hidden_local = gate_proj.shape[1]
    share = width // tensor_ways
    cols_e = out_proj.shape[1]
    cols_et = cols_e // tensor_ways
    me_e = lax.axis_index("expert")
    me_t = lax.axis_index("tensor")
    all_tok = groups * tok_count

    experts_all = groups * exp_local
    hit_src = expert_ids[:, :, None] == jnp.arange(experts_all, dtype=jnp.int32)[None, None, :]
    weights = gate_scores / jnp.sum(gate_scores, axis=1, keepdims=True)
    w_src = jnp.sum(jnp.where(hit_src, weights[:, :, None], 0.0), axis=1)
    hi = w_src.astype(jnp.bfloat16)
    rest = w_src - hi.astype(jnp.float32)
    mid = rest.astype(jnp.bfloat16)
    lo = (rest - mid.astype(jnp.float32)).astype(jnp.bfloat16)
    coded = jnp.stack([hi, mid, lo]).reshape(-1)
    heads_w = attn_heads.shape[1]
    extra = -(-coded.shape[0] // (heads_w * 8)) * 8
    coded = jnp.pad(coded, (0, extra * heads_w - coded.shape[0])).reshape(extra, heads_w)
    packet = jnp.concatenate([attn_heads, coded], axis=0)

    got = lax.all_gather(packet, "expert", axis=0, tiled=False)
    partial = jnp.einsum(
        "enh,hc->enc", got[:, :tok_count], out_proj, preferred_element_type=jnp.float32
    ).reshape(all_tok, cols_e)
    parts = got[:, tok_count:].reshape(groups, -1)[:, : 3 * tok_count * experts_all]
    parts = parts.reshape(groups, 3, tok_count, experts_all).astype(jnp.float32)
    w_all = (parts[:, 0] + parts[:, 1] + parts[:, 2]).reshape(all_tok, experts_all)
    w_mine = lax.dynamic_slice_in_dim(w_all, me_e * exp_local, exp_local, 1)
    summed = lax.psum_scatter(partial, "tensor", scatter_dimension=1, tiled=True)
    mine = lax.all_to_all(
        summed.reshape(groups, tok_count, cols_et), "expert", 0, 0, tiled=False
    )
    res_cols = lax.dynamic_index_in_dim(
        residual.reshape(tok_count, groups, tensor_ways, cols_et), me_t, 2, keepdims=False
    )
    state_ct = (jnp.transpose(res_cols, (1, 0, 2)).astype(jnp.float32) + mine).astype(
        jnp.bfloat16
    )
    state_all = lax.all_gather(state_ct, "tensor", axis=0, tiled=False)
    state = jnp.transpose(state_all, (2, 1, 0, 3)).reshape(tok_count, width)
    state_f = state.astype(jnp.float32)

    squares = jnp.sum(state_f * state_f, axis=1, keepdims=True)
    scale = lax.rsqrt(squares / width + EPS)
    state_q = lax.dynamic_slice_in_dim(state_f, me_t * share, share, 1)
    gain_q = lax.dynamic_slice_in_dim(norm_gain, me_t * share, share, 0).astype(jnp.float32)
    normed_q = (state_q * scale * gain_q).astype(jnp.bfloat16)

    slabs = lax.all_gather(normed_q, ("tensor", "expert"), axis=0, tiled=False).reshape(
        tensor_ways, all_tok, share
    )

    total = jnp.zeros((all_tok, share), jnp.float32)
    for loc in range(exp_local):
        gate = None
        upper = None
        for a in range(tensor_ways):
            x = slabs[a]
            gpart = jnp.dot(
                x, gate_proj[loc, :, a * share : (a + 1) * share].T,
                preferred_element_type=jnp.float32,
            )
            upart = jnp.dot(
                x, up_proj[loc, :, a * share : (a + 1) * share].T,
                preferred_element_type=jnp.float32,
            )
            gate = gpart if gate is None else gate + gpart
            upper = upart if upper is None else upper + upart
        act = (jax.nn.silu(gate) * upper).astype(jnp.bfloat16)
        act_all = lax.all_gather(act, "tensor", axis=1, tiled=True)
        out = jnp.dot(
            act_all, down_proj[loc], preferred_element_type=jnp.float32
        ).astype(jnp.bfloat16)
        w_tok = w_mine[:, loc][:, None]
        total = total + jnp.where(w_tok > 0, w_tok * out.astype(jnp.float32), 0.0)
    mixture = lax.psum_scatter(
        total.astype(jnp.bfloat16), "expert", scatter_dimension=0, tiled=True
    ).astype(jnp.float32)
    state_out = lax.dynamic_slice_in_dim(state_f, me_t * share, share, 1)
    return (state_out + mixture).astype(jnp.bfloat16)


def solution(mesh):
    in_specs = (
        P("expert", "tensor"),
        P("tensor", "expert"),
        P("expert", None),
        P(),
        P("expert", "tensor", None),
        P("expert", "tensor", None),
        P("expert", None, "tensor"),
        P("expert", None),
        P("expert", None),
    )
    out_specs = P("expert", "tensor")
    return jax.shard_map(
        on_device, mesh=mesh, in_specs=in_specs, out_specs=out_specs, check_vma=False
    )
```

```python
import jax
import jax.numpy as jnp
from jax import lax
from jax.sharding import PartitionSpec as P

EPS = 1e-06


def on_device(
    attn_heads,
    out_proj,
    residual,
    norm_gain,
    gate_proj,
    up_proj,
    down_proj,
    expert_ids,
    gate_scores,
):
    tok_count = residual.shape[0]
    width = residual.shape[1]
    groups = lax.axis_size("expert")
    tensor_ways = lax.axis_size("tensor")
    exp_local = gate_proj.shape[0]
    hidden_local = gate_proj.shape[1]
    share = width // tensor_ways
    cols_e = out_proj.shape[1]
    cols_et = cols_e // tensor_ways
    me_e = lax.axis_index("expert")
    me_t = lax.axis_index("tensor")
    all_tok = groups * tok_count

    experts_all = groups * exp_local
    hit_src = expert_ids[:, :, None] == jnp.arange(experts_all, dtype=jnp.int32)[None, None, :]
    weights = gate_scores / jnp.sum(gate_scores, axis=1, keepdims=True)
    w_src = jnp.sum(jnp.where(hit_src, weights[:, :, None], 0.0), axis=1)
    hi = w_src.astype(jnp.bfloat16)
    rest = w_src - hi.astype(jnp.float32)
    mid = rest.astype(jnp.bfloat16)
    lo = (rest - mid.astype(jnp.float32)).astype(jnp.bfloat16)
    coded = jnp.stack([hi, mid, lo]).reshape(-1)
    heads_w = attn_heads.shape[1]
    extra = -(-coded.shape[0] // (heads_w * 8)) * 8
    coded = jnp.pad(coded, (0, extra * heads_w - coded.shape[0])).reshape(extra, heads_w)
    packet = jnp.concatenate([attn_heads, coded], axis=0)

    got = lax.all_gather(packet, "expert", axis=0, tiled=False)
    partial = jnp.einsum(
        "enh,hc->enc", got[:, :tok_count], out_proj, preferred_element_type=jnp.float32
    ).reshape(all_tok, cols_e)
    parts = got[:, tok_count:].reshape(groups, -1)[:, : 3 * tok_count * experts_all]
    parts = parts.reshape(groups, 3, tok_count, experts_all).astype(jnp.float32)
    w_all = (parts[:, 0] + parts[:, 1] + parts[:, 2]).reshape(all_tok, experts_all)
    w_mine = lax.dynamic_slice_in_dim(w_all, me_e * exp_local, exp_local, 1)
    summed = lax.psum_scatter(partial, "tensor", scatter_dimension=1, tiled=True)
    mine = lax.all_to_all(
        summed.reshape(groups, tok_count, cols_et), "expert", 0, 0, tiled=False
    )
    res_cols = lax.dynamic_index_in_dim(
        residual.reshape(tok_count, groups, tensor_ways, cols_et), me_t, 2, keepdims=False
    )
    state_ct = (jnp.transpose(res_cols, (1, 0, 2)).astype(jnp.float32) + mine).astype(
        jnp.bfloat16
    )
    state_all = lax.all_gather(state_ct, "tensor", axis=0, tiled=False)
    state = jnp.transpose(state_all, (2, 1, 0, 3)).reshape(tok_count, width)
    state_f = state.astype(jnp.float32)

    squares = jnp.sum(state_f * state_f, axis=1, keepdims=True)
    scale = lax.rsqrt(squares / width + EPS)
    state_q = lax.dynamic_slice_in_dim(state_f, me_t * share, share, 1)
    gain_q = lax.dynamic_slice_in_dim(norm_gain, me_t * share, share, 0).astype(jnp.float32)
    normed_q = (state_q * scale * gain_q).astype(jnp.bfloat16)

    slabs = lax.all_gather(normed_q, ("tensor", "expert"), axis=0, tiled=False).reshape(
        tensor_ways, all_tok, share
    )

    total = jnp.zeros((all_tok, share), jnp.float32)
    for loc in range(exp_local):
        gate = None
        upper = None
        for a in range(tensor_ways):
            x = slabs[a]
            gpart = jnp.dot(
                x, gate_proj[loc, :, a * share : (a + 1) * share].T,
                preferred_element_type=jnp.float32,
            )
            upart = jnp.dot(
                x, up_proj[loc, :, a * share : (a + 1) * share].T,
                preferred_element_type=jnp.float32,
            )
            gate = gpart if gate is None else gate + gpart
            upper = upart if upper is None else upper + upart
        act = (jax.nn.silu(gate) * upper).astype(jnp.bfloat16)
        act_all = lax.all_gather(act, "tensor", axis=1, tiled=True)
        out = jnp.dot(
            act_all, down_proj[loc], preferred_element_type=jnp.float32
        ).astype(jnp.bfloat16)
        w_tok = w_mine[:, loc][:, None]
        total = total + jnp.where(w_tok > 0, w_tok * out.astype(jnp.float32), 0.0)
    blocks = total.reshape(groups, tok_count, share)
    mixture = lax.dynamic_index_in_dim(blocks, me_e, 0, keepdims=False)
    for s in range(1, groups):
        dest = lax.rem(me_e + s, groups)
        sent = lax.dynamic_index_in_dim(blocks, dest, 0, keepdims=False)
        perm = [(i, (i + s) % groups) for i in range(groups)]
        mixture = mixture + lax.ppermute(sent, "expert", perm)
    state_out = lax.dynamic_slice_in_dim(state_f, me_t * share, share, 1)
    return (state_out + mixture).astype(jnp.bfloat16)


def solution(mesh):
    in_specs = (
        P("expert", "tensor"),
        P("tensor", "expert"),
        P("expert", None),
        P(),
        P("expert", "tensor", None),
        P("expert", "tensor", None),
        P("expert", None, "tensor"),
        P("expert", None),
        P("expert", None),
    )
    out_specs = P("expert", "tensor")
    return jax.shard_map(
        on_device, mesh=mesh, in_specs=in_specs, out_specs=out_specs, check_vma=False
    )
```

```python
import jax
import jax.numpy as jnp
from jax import lax
from jax.sharding import PartitionSpec as P

EPS = 1e-06
EXPERT = ("ez", "ex")


def on_device(
    attn_heads,
    out_proj,
    residual,
    norm_gain,
    gate_proj,
    up_proj,
    down_proj,
    expert_ids,
    gate_scores,
):
    tok_count = residual.shape[0]
    width = residual.shape[1]
    groups = lax.axis_size(EXPERT)
    tensor_ways = lax.axis_size("tensor")
    exp_local = gate_proj.shape[0]
    hidden_local = gate_proj.shape[1]
    share = width // tensor_ways
    cols_e = out_proj.shape[1]
    cols_et = cols_e // tensor_ways
    me_e = lax.axis_index(EXPERT)
    me_t = lax.axis_index("tensor")
    all_tok = groups * tok_count

    experts_all = groups * exp_local
    hit_src = expert_ids[:, :, None] == jnp.arange(experts_all, dtype=jnp.int32)[None, None, :]
    weights = gate_scores / jnp.sum(gate_scores, axis=1, keepdims=True)
    w_src = jnp.sum(jnp.where(hit_src, weights[:, :, None], 0.0), axis=1)
    hi = w_src.astype(jnp.bfloat16)
    rest = w_src - hi.astype(jnp.float32)
    mid = rest.astype(jnp.bfloat16)
    lo = (rest - mid.astype(jnp.float32)).astype(jnp.bfloat16)
    coded = jnp.stack([hi, mid, lo]).reshape(-1)
    heads_w = attn_heads.shape[1]
    extra = -(-coded.shape[0] // (heads_w * 8)) * 8
    coded = jnp.pad(coded, (0, extra * heads_w - coded.shape[0])).reshape(extra, heads_w)
    packet = jnp.concatenate([attn_heads, coded], axis=0)

    pair = lax.all_gather(packet, "ex", axis=0, tiled=False)
    got = lax.all_gather(pair, "ez", axis=0, tiled=False).reshape(
        (groups,) + packet.shape
    )
    partial = jnp.einsum(
        "enh,hc->enc", got[:, :tok_count], out_proj, preferred_element_type=jnp.float32
    ).reshape(all_tok, cols_e)
    parts = got[:, tok_count:].reshape(groups, -1)[:, : 3 * tok_count * experts_all]
    parts = parts.reshape(groups, 3, tok_count, experts_all).astype(jnp.float32)
    w_all = (parts[:, 0] + parts[:, 1] + parts[:, 2]).reshape(all_tok, experts_all)
    w_mine = lax.dynamic_slice_in_dim(w_all, me_e * exp_local, exp_local, 1)
    summed = lax.psum_scatter(partial, "tensor", scatter_dimension=1, tiled=True)
    mine = lax.all_to_all(
        summed.reshape(groups, tok_count, cols_et), EXPERT, 0, 0, tiled=False
    )
    res_cols = lax.dynamic_index_in_dim(
        residual.reshape(tok_count, groups, tensor_ways, cols_et), me_t, 2, keepdims=False
    )
    state_ct = (jnp.transpose(res_cols, (1, 0, 2)).astype(jnp.float32) + mine).astype(
        jnp.bfloat16
    )
    state_all = lax.all_gather(state_ct, "tensor", axis=0, tiled=False)
    state = jnp.transpose(state_all, (2, 1, 0, 3)).reshape(tok_count, width)
    state_f = state.astype(jnp.float32)

    squares = jnp.sum(state_f * state_f, axis=1, keepdims=True)
    scale = lax.rsqrt(squares / width + EPS)
    state_q = lax.dynamic_slice_in_dim(state_f, me_t * share, share, 1)
    gain_q = lax.dynamic_slice_in_dim(norm_gain, me_t * share, share, 0).astype(jnp.float32)
    normed_q = (state_q * scale * gain_q).astype(jnp.bfloat16)

    slabs = lax.all_gather(normed_q, ("tensor",) + EXPERT, axis=0, tiled=False).reshape(
        tensor_ways, all_tok, share
    )

    total = jnp.zeros((all_tok, share), jnp.float32)
    for loc in range(exp_local):
        gate = None
        upper = None
        for a in range(tensor_ways):
            x = slabs[a]
            gpart = jnp.dot(
                x, gate_proj[loc, :, a * share : (a + 1) * share].T,
                preferred_element_type=jnp.float32,
            )
            upart = jnp.dot(
                x, up_proj[loc, :, a * share : (a + 1) * share].T,
                preferred_element_type=jnp.float32,
            )
            gate = gpart if gate is None else gate + gpart
            upper = upart if upper is None else upper + upart
        act = (jax.nn.silu(gate) * upper).astype(jnp.bfloat16)
        act_all = lax.all_gather(act, "tensor", axis=1, tiled=True)
        out = jnp.dot(
            act_all, down_proj[loc], preferred_element_type=jnp.float32
        ).astype(jnp.bfloat16)
        w_tok = w_mine[:, loc][:, None]
        total = total + jnp.where(w_tok > 0, w_tok * out.astype(jnp.float32), 0.0)
    near = lax.axis_size("ex")
    far = groups // near
    by_x = jnp.transpose(
        total.astype(jnp.bfloat16).reshape(far, near, tok_count, share), (1, 0, 2, 3)
    )
    halves = lax.psum_scatter(by_x, "ex", scatter_dimension=0, tiled=True)
    mixture = lax.psum_scatter(
        halves.reshape(far, tok_count, share), "ez", scatter_dimension=0, tiled=True
    )
    mixture = mixture.reshape(tok_count, share).astype(jnp.float32)
    state_out = lax.dynamic_slice_in_dim(state_f, me_t * share, share, 1)
    return (state_out + mixture).astype(jnp.bfloat16)


def solution(mesh):
    in_specs = (
        P(EXPERT, "tensor"),
        P("tensor", EXPERT),
        P(EXPERT, None),
        P(),
        P(EXPERT, "tensor", None),
        P(EXPERT, "tensor", None),
        P(EXPERT, None, "tensor"),
        P(EXPERT, None),
        P(EXPERT, None),
    )
    out_specs = P(EXPERT, "tensor")
    devices = mesh.devices
    near = 2 if devices.shape[0] % 2 == 0 else 1
    split = jax.sharding.Mesh(
        devices.reshape(devices.shape[0] // near, near, devices.shape[1]),
        ("ez", "ex", "tensor"),
    )
    return jax.shard_map(
        on_device, mesh=split, in_specs=in_specs, out_specs=out_specs, check_vma=False
    )
```

```python
import jax
import jax.numpy as jnp
from jax import lax
from jax.sharding import PartitionSpec as P

EPS = 1e-06


def on_device(
    attn_heads,
    out_proj,
    residual,
    norm_gain,
    gate_proj,
    up_proj,
    down_proj,
    expert_ids,
    gate_scores,
):
    tok_count = residual.shape[0]
    width = residual.shape[1]
    groups = lax.axis_size("expert")
    tensor_ways = lax.axis_size("tensor")
    exp_local = gate_proj.shape[0]
    hidden_local = gate_proj.shape[1]
    share = width // tensor_ways
    cols_e = out_proj.shape[1]
    cols_et = cols_e // tensor_ways
    me_e = lax.axis_index("expert")
    me_t = lax.axis_index("tensor")
    all_tok = groups * tok_count

    experts_all = groups * exp_local
    hit_src = expert_ids[:, :, None] == jnp.arange(experts_all, dtype=jnp.int32)[None, None, :]
    weights = gate_scores / jnp.sum(gate_scores, axis=1, keepdims=True)
    w_src = jnp.sum(jnp.where(hit_src, weights[:, :, None], 0.0), axis=1)
    hi = w_src.astype(jnp.bfloat16)
    rest = w_src - hi.astype(jnp.float32)
    mid = rest.astype(jnp.bfloat16)
    lo = (rest - mid.astype(jnp.float32)).astype(jnp.bfloat16)
    coded = jnp.stack([hi, mid, lo]).reshape(-1)
    heads_w = attn_heads.shape[1]
    extra = -(-coded.shape[0] // (heads_w * 8)) * 8
    coded = jnp.pad(coded, (0, extra * heads_w - coded.shape[0])).reshape(extra, heads_w)
    packet = jnp.concatenate([attn_heads, coded], axis=0)

    got = lax.all_gather(packet, "expert", axis=0, tiled=False)
    partial = jnp.einsum(
        "enh,hc->enc", got[:, :tok_count], out_proj, preferred_element_type=jnp.float32
    ).reshape(all_tok, cols_e)
    parts = got[:, tok_count:].reshape(groups, -1)[:, : 3 * tok_count * experts_all]
    parts = parts.reshape(groups, 3, tok_count, experts_all).astype(jnp.float32)
    w_all = (parts[:, 0] + parts[:, 1] + parts[:, 2]).reshape(all_tok, experts_all)
    w_mine = lax.dynamic_slice_in_dim(w_all, me_e * exp_local, exp_local, 1)
    summed = lax.psum_scatter(partial, "tensor", scatter_dimension=1, tiled=True)
    mine = lax.all_to_all(
        summed.reshape(groups, tok_count, cols_et), "expert", 0, 0, tiled=False
    )
    res_cols = lax.dynamic_index_in_dim(
        residual.reshape(tok_count, groups, tensor_ways, cols_et), me_t, 2, keepdims=False
    )
    state_ct = (jnp.transpose(res_cols, (1, 0, 2)).astype(jnp.float32) + mine).astype(
        jnp.bfloat16
    )
    state_all = lax.all_gather(state_ct, "tensor", axis=0, tiled=False)
    state = jnp.transpose(state_all, (2, 1, 0, 3)).reshape(tok_count, width)
    state_f = state.astype(jnp.float32)

    squares = jnp.sum(state_f * state_f, axis=1, keepdims=True)
    scale = lax.rsqrt(squares / width + EPS)
    state_q = lax.dynamic_slice_in_dim(state_f, me_t * share, share, 1)
    gain_q = lax.dynamic_slice_in_dim(norm_gain, me_t * share, share, 0).astype(jnp.float32)
    normed_q = (state_q * scale * gain_q).astype(jnp.bfloat16)

    slabs = lax.all_gather(normed_q, ("tensor", "expert"), axis=0, tiled=False).reshape(
        tensor_ways, all_tok, share
    )

    total = jnp.zeros((all_tok, share), jnp.float32)
    for loc in range(exp_local):
        gate = None
        upper = None
        for a in range(tensor_ways):
            x = slabs[a]
            gpart = jnp.dot(
                x, gate_proj[loc, :, a * share : (a + 1) * share].T,
                preferred_element_type=jnp.float32,
            )
            upart = jnp.dot(
                x, up_proj[loc, :, a * share : (a + 1) * share].T,
                preferred_element_type=jnp.float32,
            )
            gate = gpart if gate is None else gate + gpart
            upper = upart if upper is None else upper + upart
        act = (jax.nn.silu(gate) * upper).astype(jnp.bfloat16)
        act_all = lax.all_gather(act, "tensor", axis=1, tiled=True)
        out = jnp.dot(
            act_all, down_proj[loc], preferred_element_type=jnp.float32
        ).astype(jnp.bfloat16)
        w_tok = w_mine[:, loc][:, None]
        total = total + jnp.where(w_tok > 0, w_tok * out.astype(jnp.float32), 0.0)
    near = 2 if groups % 2 == 0 else 1
    far = groups // near
    pairs = [[z * near + x for x in range(near)] for z in range(far)]
    lines = [[z * near + x for z in range(far)] for x in range(near)]
    halves = lax.psum_scatter(
        total.astype(jnp.bfloat16).reshape(far, near * tok_count, share), "expert",
        scatter_dimension=0, tiled=True, axis_index_groups=lines,
    )
    mixture = lax.psum_scatter(
        halves.reshape(near * tok_count, share), "expert", scatter_dimension=0,
        tiled=True, axis_index_groups=pairs,
    )
    mixture = mixture.astype(jnp.float32)
    state_out = lax.dynamic_slice_in_dim(state_f, me_t * share, share, 1)
    return (state_out + mixture).astype(jnp.bfloat16)


def solution(mesh):
    in_specs = (
        P("expert", "tensor"),
        P("tensor", "expert"),
        P("expert", None),
        P(),
        P("expert", "tensor", None),
        P("expert", "tensor", None),
        P("expert", None, "tensor"),
        P("expert", None),
        P("expert", None),
    )
    out_specs = P("expert", "tensor")
    return jax.shard_map(
        on_device, mesh=mesh, in_specs=in_specs, out_specs=out_specs, check_vma=False
    )
```

```python
import jax
import jax.numpy as jnp
from jax import lax
from jax.sharding import PartitionSpec as P
from jax.experimental.layout import Layout, with_layout_constraint

EPS = 1e-06


def on_device(
    attn_heads,
    out_proj,
    residual,
    norm_gain,
    gate_proj,
    up_proj,
    down_proj,
    expert_ids,
    gate_scores,
):
    tok_count = residual.shape[0]
    width = residual.shape[1]
    groups = lax.axis_size("expert")
    tensor_ways = lax.axis_size("tensor")
    exp_local = gate_proj.shape[0]
    hidden_local = gate_proj.shape[1]
    share = width // tensor_ways
    cols_e = out_proj.shape[1]
    cols_et = cols_e // tensor_ways
    me_e = lax.axis_index("expert")
    me_t = lax.axis_index("tensor")
    all_tok = groups * tok_count

    experts_all = groups * exp_local
    hit_src = expert_ids[:, :, None] == jnp.arange(experts_all, dtype=jnp.int32)[None, None, :]
    weights = gate_scores / jnp.sum(gate_scores, axis=1, keepdims=True)
    w_src = jnp.sum(jnp.where(hit_src, weights[:, :, None], 0.0), axis=1)
    hi = w_src.astype(jnp.bfloat16)
    rest = w_src - hi.astype(jnp.float32)
    mid = rest.astype(jnp.bfloat16)
    lo = (rest - mid.astype(jnp.float32)).astype(jnp.bfloat16)
    coded = jnp.stack([hi, mid, lo]).reshape(-1)
    heads_w = attn_heads.shape[1]
    extra = -(-coded.shape[0] // (heads_w * 8)) * 8
    coded = jnp.pad(coded, (0, extra * heads_w - coded.shape[0])).reshape(extra, heads_w)
    packet = jnp.concatenate([attn_heads, coded], axis=0)

    got = lax.all_gather(packet, "expert", axis=0, tiled=False)
    partial = jnp.einsum(
        "enh,hc->enc", got[:, :tok_count], out_proj, preferred_element_type=jnp.float32
    ).reshape(all_tok, cols_e)
    parts = got[:, tok_count:].reshape(groups, -1)[:, : 3 * tok_count * experts_all]
    parts = parts.reshape(groups, 3, tok_count, experts_all).astype(jnp.float32)
    w_all = (parts[:, 0] + parts[:, 1] + parts[:, 2]).reshape(all_tok, experts_all)
    w_mine = lax.dynamic_slice_in_dim(w_all, me_e * exp_local, exp_local, 1)
    summed = lax.psum_scatter(partial, "tensor", scatter_dimension=1, tiled=True)
    mine = lax.all_to_all(
        summed.reshape(groups, tok_count, cols_et), "expert", 0, 0, tiled=False
    )
    res_cols = lax.dynamic_index_in_dim(
        residual.reshape(tok_count, groups, tensor_ways, cols_et), me_t, 2, keepdims=False
    )
    state_ct = (jnp.transpose(res_cols, (1, 0, 2)).astype(jnp.float32) + mine).astype(
        jnp.bfloat16
    )
    state_all = lax.all_gather(state_ct, "tensor", axis=0, tiled=False)
    state = jnp.transpose(state_all, (2, 1, 0, 3)).reshape(tok_count, width)
    state_f = state.astype(jnp.float32)

    squares = jnp.sum(state_f * state_f, axis=1, keepdims=True)
    scale = lax.rsqrt(squares / width + EPS)
    state_q = lax.dynamic_slice_in_dim(state_f, me_t * share, share, 1)
    gain_q = lax.dynamic_slice_in_dim(norm_gain, me_t * share, share, 0).astype(jnp.float32)
    normed_q = (state_q * scale * gain_q).astype(jnp.bfloat16)

    normed_q = with_layout_constraint(normed_q, Layout(major_to_minor=(0, 1)))
    slabs = lax.all_gather(normed_q, ("tensor", "expert"), axis=0, tiled=False)
    slabs = slabs.reshape(tensor_ways, all_tok, share)

    total = jnp.zeros((all_tok, share), jnp.float32)
    for loc in range(exp_local):
        gate = None
        upper = None
        for a in range(tensor_ways):
            x = slabs[a]
            gpart = jnp.dot(
                x, gate_proj[loc, :, a * share : (a + 1) * share].T,
                preferred_element_type=jnp.float32,
            )
            upart = jnp.dot(
                x, up_proj[loc, :, a * share : (a + 1) * share].T,
                preferred_element_type=jnp.float32,
            )
            gate = gpart if gate is None else gate + gpart
            upper = upart if upper is None else upper + upart
        act = (jax.nn.silu(gate) * upper).astype(jnp.bfloat16)
        act_all = lax.all_gather(act, "tensor", axis=1, tiled=True)
        out = jnp.dot(
            act_all, down_proj[loc], preferred_element_type=jnp.float32
        ).astype(jnp.bfloat16)
        w_tok = w_mine[:, loc][:, None]
        total = total + jnp.where(w_tok > 0, w_tok * out.astype(jnp.float32), 0.0)
    near = 2 if groups % 2 == 0 else 1
    far = groups // near
    pairs = [[z * near + x for x in range(near)] for z in range(far)]
    lines = [[z * near + x for z in range(far)] for x in range(near)]
    halves = lax.psum_scatter(
        total.astype(jnp.bfloat16).reshape(far, near * tok_count, share), "expert",
        scatter_dimension=0, tiled=True, axis_index_groups=lines,
    )
    mixture = lax.psum_scatter(
        halves.reshape(near * tok_count, share), "expert", scatter_dimension=0,
        tiled=True, axis_index_groups=pairs,
    )
    mixture = mixture.astype(jnp.float32)
    state_out = lax.dynamic_slice_in_dim(state_f, me_t * share, share, 1)
    return (state_out + mixture).astype(jnp.bfloat16)


def solution(mesh):
    in_specs = (
        P("expert", "tensor"),
        P("tensor", "expert"),
        P("expert", None),
        P(),
        P("expert", "tensor", None),
        P("expert", "tensor", None),
        P("expert", None, "tensor"),
        P("expert", None),
        P("expert", None),
    )
    out_specs = P("expert", "tensor")
    return jax.shard_map(
        on_device, mesh=mesh, in_specs=in_specs, out_specs=out_specs, check_vma=False
    )
```

```python
import jax
import jax.numpy as jnp
from jax import lax
from jax.sharding import PartitionSpec as P
from jax.experimental.layout import Layout, with_layout_constraint

EPS = 1e-06


def on_device(
    attn_heads,
    out_proj,
    residual,
    norm_gain,
    gate_proj,
    up_proj,
    down_proj,
    expert_ids,
    gate_scores,
):
    tok_count = residual.shape[0]
    width = residual.shape[1]
    groups = lax.axis_size("expert")
    tensor_ways = lax.axis_size("tensor")
    exp_local = gate_proj.shape[0]
    hidden_local = gate_proj.shape[1]
    share = width // tensor_ways
    cols_e = out_proj.shape[1]
    cols_et = cols_e // tensor_ways
    me_e = lax.axis_index("expert")
    me_t = lax.axis_index("tensor")
    all_tok = groups * tok_count

    experts_all = groups * exp_local
    hit_src = expert_ids[:, :, None] == jnp.arange(experts_all, dtype=jnp.int32)[None, None, :]
    weights = gate_scores / jnp.sum(gate_scores, axis=1, keepdims=True)
    w_src = jnp.sum(jnp.where(hit_src, weights[:, :, None], 0.0), axis=1)
    hi = w_src.astype(jnp.bfloat16)
    rest = w_src - hi.astype(jnp.float32)
    mid = rest.astype(jnp.bfloat16)
    lo = (rest - mid.astype(jnp.float32)).astype(jnp.bfloat16)
    coded = jnp.stack([hi, mid, lo]).reshape(-1)
    heads_w = attn_heads.shape[1]
    extra = -(-coded.shape[0] // (heads_w * 8)) * 8
    coded = jnp.pad(coded, (0, extra * heads_w - coded.shape[0])).reshape(extra, heads_w)
    packet = jnp.concatenate([attn_heads, coded], axis=0)

    got = lax.all_gather(packet, "expert", axis=0, tiled=False)
    partial = jnp.einsum(
        "enh,hc->enc", got[:, :tok_count], out_proj, preferred_element_type=jnp.float32
    ).reshape(all_tok, cols_e)
    parts = got[:, tok_count:].reshape(groups, -1)[:, : 3 * tok_count * experts_all]
    parts = parts.reshape(groups, 3, tok_count, experts_all).astype(jnp.float32)
    w_all = (parts[:, 0] + parts[:, 1] + parts[:, 2]).reshape(all_tok, experts_all)
    w_mine = lax.dynamic_slice_in_dim(w_all, me_e * exp_local, exp_local, 1)
    cores = 2 if tensor_ways % 2 == 0 else 1
    chips = tensor_ways // cores
    on_chip = [[y * cores + c for c in range(cores)] for y in range(chips)]
    across = [[y * cores + c for y in range(chips)] for c in range(cores)]
    blk_of = [(t % cores) * chips + t // cores for t in range(tensor_ways)]
    holder = [blk_of.index(b) for b in range(tensor_ways)]
    blk = lax.rem(me_t, cores) * chips + me_t // cores
    halves_t = lax.psum_scatter(
        partial, "tensor", scatter_dimension=1, tiled=True, axis_index_groups=on_chip
    )
    summed = lax.psum_scatter(
        halves_t, "tensor", scatter_dimension=1, tiled=True, axis_index_groups=across
    )
    mine = lax.all_to_all(
        summed.reshape(groups, tok_count, cols_et), "expert", 0, 0, tiled=False
    )
    res_cols = lax.dynamic_index_in_dim(
        residual.reshape(tok_count, groups, tensor_ways, cols_et), blk, 2, keepdims=False
    )
    state_ct = (jnp.transpose(res_cols, (1, 0, 2)).astype(jnp.float32) + mine).astype(
        jnp.bfloat16
    )
    state_all = lax.all_gather(state_ct, "tensor", axis=0, tiled=False)
    state_all = jnp.stack([state_all[h] for h in holder])
    state = jnp.transpose(state_all, (2, 1, 0, 3)).reshape(tok_count, width)
    state_f = state.astype(jnp.float32)

    squares = jnp.sum(state_f * state_f, axis=1, keepdims=True)
    scale = lax.rsqrt(squares / width + EPS)
    state_q = lax.dynamic_slice_in_dim(state_f, me_t * share, share, 1)
    gain_q = lax.dynamic_slice_in_dim(norm_gain, me_t * share, share, 0).astype(jnp.float32)
    normed_q = (state_q * scale * gain_q).astype(jnp.bfloat16)

    normed_q = with_layout_constraint(normed_q, Layout(major_to_minor=(0, 1)))
    slabs = lax.all_gather(normed_q, ("tensor", "expert"), axis=0, tiled=False)
    slabs = slabs.reshape(tensor_ways, all_tok, share)

    total = jnp.zeros((all_tok, share), jnp.float32)
    for loc in range(exp_local):
        gate = None
        upper = None
        for a in range(tensor_ways):
            x = slabs[a]
            gpart = jnp.dot(
                x, gate_proj[loc, :, a * share : (a + 1) * share].T,
                preferred_element_type=jnp.float32,
            )
            upart = jnp.dot(
                x, up_proj[loc, :, a * share : (a + 1) * share].T,
                preferred_element_type=jnp.float32,
            )
            gate = gpart if gate is None else gate + gpart
            upper = upart if upper is None else upper + upart
        act = (jax.nn.silu(gate) * upper).astype(jnp.bfloat16)
        act_all = lax.all_gather(act, "tensor", axis=1, tiled=True)
        out = jnp.dot(
            act_all, down_proj[loc], preferred_element_type=jnp.float32
        ).astype(jnp.bfloat16)
        w_tok = w_mine[:, loc][:, None]
        total = total + jnp.where(w_tok > 0, w_tok * out.astype(jnp.float32), 0.0)
    near = 2 if groups % 2 == 0 else 1
    far = groups // near
    pairs = [[z * near + x for x in range(near)] for z in range(far)]
    lines = [[z * near + x for z in range(far)] for x in range(near)]
    halves = lax.psum_scatter(
        total.astype(jnp.bfloat16).reshape(far, near * tok_count, share), "expert",
        scatter_dimension=0, tiled=True, axis_index_groups=lines,
    )
    mixture = lax.psum_scatter(
        halves.reshape(near * tok_count, share), "expert", scatter_dimension=0,
        tiled=True, axis_index_groups=pairs,
    )
    mixture = mixture.astype(jnp.float32)
    state_out = lax.dynamic_slice_in_dim(state_f, me_t * share, share, 1)
    return (state_out + mixture).astype(jnp.bfloat16)


def solution(mesh):
    in_specs = (
        P("expert", "tensor"),
        P("tensor", "expert"),
        P("expert", None),
        P(),
        P("expert", "tensor", None),
        P("expert", "tensor", None),
        P("expert", None, "tensor"),
        P("expert", None),
        P("expert", None),
    )
    out_specs = P("expert", "tensor")
    return jax.shard_map(
        on_device, mesh=mesh, in_specs=in_specs, out_specs=out_specs, check_vma=False
    )
```

```python
import jax
import jax.numpy as jnp
from jax import lax
from jax.sharding import PartitionSpec as P
from jax.experimental.layout import Layout, with_layout_constraint

EPS = 1e-06


def on_device(
    attn_heads,
    out_proj,
    residual,
    norm_gain,
    gate_proj,
    up_proj,
    down_proj,
    expert_ids,
    gate_scores,
):
    tok_count = residual.shape[0]
    width = residual.shape[1]
    groups = lax.axis_size("expert")
    tensor_ways = lax.axis_size("tensor")
    exp_local = gate_proj.shape[0]
    hidden_local = gate_proj.shape[1]
    share = width // tensor_ways
    cols_e = out_proj.shape[1]
    cols_et = cols_e // tensor_ways
    me_e = lax.axis_index("expert")
    me_t = lax.axis_index("tensor")
    all_tok = groups * tok_count

    experts_all = groups * exp_local
    hit_src = expert_ids[:, :, None] == jnp.arange(experts_all, dtype=jnp.int32)[None, None, :]
    weights = gate_scores / jnp.sum(gate_scores, axis=1, keepdims=True)
    w_src = jnp.sum(jnp.where(hit_src, weights[:, :, None], 0.0), axis=1)
    hi = w_src.astype(jnp.bfloat16)
    rest = w_src - hi.astype(jnp.float32)
    mid = rest.astype(jnp.bfloat16)
    lo = (rest - mid.astype(jnp.float32)).astype(jnp.bfloat16)
    coded = jnp.stack([hi, mid, lo]).reshape(-1)
    heads_w = attn_heads.shape[1]
    extra = -(-coded.shape[0] // (heads_w * 8)) * 8
    coded = jnp.pad(coded, (0, extra * heads_w - coded.shape[0])).reshape(extra, heads_w)
    packet = jnp.concatenate([attn_heads, coded], axis=0)

    near = 2 if groups % 2 == 0 else 1
    far = groups // near
    pairs = [[z * near + x for x in range(near)] for z in range(far)]
    lines = [[z * near + x for z in range(far)] for x in range(near)]
    along_z = lax.all_gather(packet, "expert", axis=0, tiled=False, axis_index_groups=lines)
    got = lax.all_gather(along_z, "expert", axis=0, tiled=False, axis_index_groups=pairs)
    got = jnp.transpose(got, (1, 0, 2, 3)).reshape((groups,) + packet.shape)
    partial = jnp.einsum(
        "enh,hc->enc", got[:, :tok_count], out_proj, preferred_element_type=jnp.float32
    ).reshape(all_tok, cols_e)
    parts = got[:, tok_count:].reshape(groups, -1)[:, : 3 * tok_count * experts_all]
    parts = parts.reshape(groups, 3, tok_count, experts_all).astype(jnp.float32)
    w_all = (parts[:, 0] + parts[:, 1] + parts[:, 2]).reshape(all_tok, experts_all)
    w_mine = lax.dynamic_slice_in_dim(w_all, me_e * exp_local, exp_local, 1)
    summed = lax.psum_scatter(partial, "tensor", scatter_dimension=1, tiled=True)
    mine = lax.all_to_all(
        summed.reshape(groups, tok_count, cols_et), "expert", 0, 0, tiled=False
    )
    res_cols = lax.dynamic_index_in_dim(
        residual.reshape(tok_count, groups, tensor_ways, cols_et), me_t, 2, keepdims=False
    )
    state_ct = (jnp.transpose(res_cols, (1, 0, 2)).astype(jnp.float32) + mine).astype(
        jnp.bfloat16
    )
    state_all = lax.all_gather(state_ct, "tensor", axis=0, tiled=False)
    state = jnp.transpose(state_all, (2, 1, 0, 3)).reshape(tok_count, width)
    state_f = state.astype(jnp.float32)

    squares = jnp.sum(state_f * state_f, axis=1, keepdims=True)
    scale = lax.rsqrt(squares / width + EPS)
    state_q = lax.dynamic_slice_in_dim(state_f, me_t * share, share, 1)
    gain_q = lax.dynamic_slice_in_dim(norm_gain, me_t * share, share, 0).astype(jnp.float32)
    normed_q = (state_q * scale * gain_q).astype(jnp.bfloat16)

    normed_q = with_layout_constraint(normed_q, Layout(major_to_minor=(0, 1)))
    slabs = lax.all_gather(normed_q, ("tensor", "expert"), axis=0, tiled=False)
    slabs = slabs.reshape(tensor_ways, all_tok, share)

    total = jnp.zeros((all_tok, share), jnp.float32)
    for loc in range(exp_local):
        gate = None
        upper = None
        for a in range(tensor_ways):
            x = slabs[a]
            gpart = jnp.dot(
                x, gate_proj[loc, :, a * share : (a + 1) * share].T,
                preferred_element_type=jnp.float32,
            )
            upart = jnp.dot(
                x, up_proj[loc, :, a * share : (a + 1) * share].T,
                preferred_element_type=jnp.float32,
            )
            gate = gpart if gate is None else gate + gpart
            upper = upart if upper is None else upper + upart
        act = (jax.nn.silu(gate) * upper).astype(jnp.bfloat16)
        act_all = lax.all_gather(act, "tensor", axis=1, tiled=True)
        out = jnp.dot(
            act_all, down_proj[loc], preferred_element_type=jnp.float32
        ).astype(jnp.bfloat16)
        w_tok = w_mine[:, loc][:, None]
        total = total + jnp.where(w_tok > 0, w_tok * out.astype(jnp.float32), 0.0)
    halves = lax.psum_scatter(
        total.astype(jnp.bfloat16).reshape(far, near * tok_count, share), "expert",
        scatter_dimension=0, tiled=True, axis_index_groups=lines,
    )
    mixture = lax.psum_scatter(
        halves.reshape(near * tok_count, share), "expert", scatter_dimension=0,
        tiled=True, axis_index_groups=pairs,
    )
    mixture = mixture.astype(jnp.float32)
    state_out = lax.dynamic_slice_in_dim(state_f, me_t * share, share, 1)
    return (state_out + mixture).astype(jnp.bfloat16)


def solution(mesh):
    in_specs = (
        P("expert", "tensor"),
        P("tensor", "expert"),
        P("expert", None),
        P(),
        P("expert", "tensor", None),
        P("expert", "tensor", None),
        P("expert", None, "tensor"),
        P("expert", None),
        P("expert", None),
    )
    out_specs = P("expert", "tensor")
    return jax.shard_map(
        on_device, mesh=mesh, in_specs=in_specs, out_specs=out_specs, check_vma=False
    )
```

```python
import jax
import jax.numpy as jnp
from jax import lax
from jax.sharding import PartitionSpec as P
from jax.experimental.layout import Layout, with_layout_constraint

EPS = 1e-06


def on_device(
    attn_heads,
    out_proj,
    residual,
    norm_gain,
    gate_proj,
    up_proj,
    down_proj,
    expert_ids,
    gate_scores,
):
    tok_count = residual.shape[0]
    width = residual.shape[1]
    groups = lax.axis_size("expert")
    tensor_ways = lax.axis_size("tensor")
    exp_local = gate_proj.shape[0]
    hidden_local = gate_proj.shape[1]
    share = width // tensor_ways
    cols_e = out_proj.shape[1]
    cols_et = cols_e // tensor_ways
    me_e = lax.axis_index("expert")
    me_t = lax.axis_index("tensor")
    all_tok = groups * tok_count

    experts_all = groups * exp_local
    hit_src = expert_ids[:, :, None] == jnp.arange(experts_all, dtype=jnp.int32)[None, None, :]
    weights = gate_scores / jnp.sum(gate_scores, axis=1, keepdims=True)
    w_src = jnp.sum(jnp.where(hit_src, weights[:, :, None], 0.0), axis=1)
    hi = w_src.astype(jnp.bfloat16)
    rest = w_src - hi.astype(jnp.float32)
    mid = rest.astype(jnp.bfloat16)
    lo = (rest - mid.astype(jnp.float32)).astype(jnp.bfloat16)
    coded = jnp.stack([hi, mid, lo]).reshape(-1)
    heads_w = attn_heads.shape[1]
    extra = -(-coded.shape[0] // (heads_w * 8)) * 8
    coded = jnp.pad(coded, (0, extra * heads_w - coded.shape[0])).reshape(extra, heads_w)
    packet = jnp.concatenate([attn_heads, coded], axis=0)

    got = lax.all_gather(packet, "expert", axis=0, tiled=False)
    partial = jnp.einsum(
        "enh,hc->enc", got[:, :tok_count], out_proj, preferred_element_type=jnp.float32
    ).reshape(all_tok, cols_e)
    parts = got[:, tok_count:].reshape(groups, -1)[:, : 3 * tok_count * experts_all]
    parts = parts.reshape(groups, 3, tok_count, experts_all).astype(jnp.float32)
    w_all = (parts[:, 0] + parts[:, 1] + parts[:, 2]).reshape(all_tok, experts_all)
    w_mine = lax.dynamic_slice_in_dim(w_all, me_e * exp_local, exp_local, 1)
    summed = lax.psum_scatter(partial, "tensor", scatter_dimension=1, tiled=True)
    res_out = lax.dynamic_index_in_dim(
        residual.reshape(tok_count, groups, tensor_ways, cols_et), me_t, 2, keepdims=False
    )
    res_in = lax.all_to_all(jnp.transpose(res_out, (1, 0, 2)), "expert", 0, 0, tiled=False)
    state_slab = (
        res_in.astype(jnp.float32) + summed.reshape(groups, tok_count, cols_et)
    ).astype(jnp.bfloat16)
    state_ct = lax.all_to_all(state_slab, "expert", 0, 0, tiled=False)
    state_all = lax.all_gather(state_ct, "tensor", axis=0, tiled=False)
    state = jnp.transpose(state_all, (2, 1, 0, 3)).reshape(tok_count, width)
    state_f = state.astype(jnp.float32)

    squares = jnp.sum(state_f * state_f, axis=1, keepdims=True)
    scale = lax.rsqrt(squares / width + EPS)
    state_q = lax.dynamic_slice_in_dim(state_f, me_t * share, share, 1)
    gain_q = lax.dynamic_slice_in_dim(norm_gain, me_t * share, share, 0).astype(jnp.float32)
    normed_q = (state_q * scale * gain_q).astype(jnp.bfloat16)

    normed_q = with_layout_constraint(normed_q, Layout(major_to_minor=(0, 1)))
    slabs = lax.all_gather(normed_q, ("tensor", "expert"), axis=0, tiled=False)
    slabs = slabs.reshape(tensor_ways, all_tok, share)

    total = jnp.zeros((all_tok, share), jnp.float32)
    for loc in range(exp_local):
        gate = None
        upper = None
        for a in range(tensor_ways):
            x = slabs[a]
            gpart = jnp.dot(
                x, gate_proj[loc, :, a * share : (a + 1) * share].T,
                preferred_element_type=jnp.float32,
            )
            upart = jnp.dot(
                x, up_proj[loc, :, a * share : (a + 1) * share].T,
                preferred_element_type=jnp.float32,
            )
            gate = gpart if gate is None else gate + gpart
            upper = upart if upper is None else upper + upart
        act = (jax.nn.silu(gate) * upper).astype(jnp.bfloat16)
        act_all = lax.all_gather(act, "tensor", axis=1, tiled=True)
        out = jnp.dot(
            act_all, down_proj[loc], preferred_element_type=jnp.float32
        ).astype(jnp.bfloat16)
        w_tok = w_mine[:, loc][:, None]
        total = total + jnp.where(w_tok > 0, w_tok * out.astype(jnp.float32), 0.0)
    near = 2 if groups % 2 == 0 else 1
    far = groups // near
    pairs = [[z * near + x for x in range(near)] for z in range(far)]
    lines = [[z * near + x for z in range(far)] for x in range(near)]
    halves = lax.psum_scatter(
        total.astype(jnp.bfloat16).reshape(far, near * tok_count, share), "expert",
        scatter_dimension=0, tiled=True, axis_index_groups=lines,
    )
    mixture = lax.psum_scatter(
        halves.reshape(near * tok_count, share), "expert", scatter_dimension=0,
        tiled=True, axis_index_groups=pairs,
    )
    mixture = mixture.astype(jnp.float32)
    state_out = lax.dynamic_slice_in_dim(state_f, me_t * share, share, 1)
    return (state_out + mixture).astype(jnp.bfloat16)


def solution(mesh):
    in_specs = (
        P("expert", "tensor"),
        P("tensor", "expert"),
        P("expert", None),
        P(),
        P("expert", "tensor", None),
        P("expert", "tensor", None),
        P("expert", None, "tensor"),
        P("expert", None),
        P("expert", None),
    )
    out_specs = P("expert", "tensor")
    return jax.shard_map(
        on_device, mesh=mesh, in_specs=in_specs, out_specs=out_specs, check_vma=False
    )
```

```python
import jax
import jax.numpy as jnp
from jax import lax
from jax.sharding import PartitionSpec as P
from jax.experimental.layout import Layout, with_layout_constraint

EPS = 1e-06


def on_device(
    attn_heads,
    out_proj,
    residual,
    norm_gain,
    gate_proj,
    up_proj,
    down_proj,
    expert_ids,
    gate_scores,
):
    tok_count = residual.shape[0]
    width = residual.shape[1]
    groups = lax.axis_size("expert")
    tensor_ways = lax.axis_size("tensor")
    exp_local = gate_proj.shape[0]
    hidden_local = gate_proj.shape[1]
    share = width // tensor_ways
    cols_e = out_proj.shape[1]
    cols_et = cols_e // tensor_ways
    me_e = lax.axis_index("expert")
    me_t = lax.axis_index("tensor")
    all_tok = groups * tok_count

    experts_all = groups * exp_local
    hit_src = expert_ids[:, :, None] == jnp.arange(experts_all, dtype=jnp.int32)[None, None, :]
    weights = gate_scores / jnp.sum(gate_scores, axis=1, keepdims=True)
    w_src = jnp.sum(jnp.where(hit_src, weights[:, :, None], 0.0), axis=1)
    hi = w_src.astype(jnp.bfloat16)
    rest = w_src - hi.astype(jnp.float32)
    mid = rest.astype(jnp.bfloat16)
    lo = (rest - mid.astype(jnp.float32)).astype(jnp.bfloat16)
    coded = jnp.stack([hi, mid, lo]).reshape(-1)
    heads_w = attn_heads.shape[1]
    extra = -(-coded.shape[0] // (heads_w * 8)) * 8
    coded = jnp.pad(coded, (0, extra * heads_w - coded.shape[0])).reshape(extra, heads_w)
    packet = jnp.concatenate([attn_heads, coded], axis=0)

    got = lax.all_gather(packet, "expert", axis=0, tiled=False)
    partial = jnp.einsum(
        "enh,hc->enc", got[:, :tok_count], out_proj, preferred_element_type=jnp.float32
    ).reshape(all_tok, cols_e)
    parts = got[:, tok_count:].reshape(groups, -1)[:, : 3 * tok_count * experts_all]
    parts = parts.reshape(groups, 3, tok_count, experts_all).astype(jnp.float32)
    w_all = (parts[:, 0] + parts[:, 1] + parts[:, 2]).reshape(all_tok, experts_all)
    w_mine = lax.dynamic_slice_in_dim(w_all, me_e * exp_local, exp_local, 1)
    summed = lax.psum_scatter(partial, "tensor", scatter_dimension=1, tiled=True)
    res_out = lax.dynamic_index_in_dim(
        residual.reshape(tok_count, groups, tensor_ways, cols_et), me_t, 2, keepdims=False
    )
    res_in = lax.all_to_all(jnp.transpose(res_out, (1, 0, 2)), "expert", 0, 0, tiled=False)
    state_slab = (
        res_in.astype(jnp.float32) + summed.reshape(groups, tok_count, cols_et)
    ).astype(jnp.bfloat16)
    state_ct = lax.all_to_all(state_slab, "expert", 0, 0, tiled=False)
    state_all = lax.all_gather(state_ct, "tensor", axis=0, tiled=False)
    state_sq = state_all.astype(jnp.float32)

    squares = jnp.sum(state_sq * state_sq, axis=(0, 1, 3))[:, None]
    scale = lax.rsqrt(squares / width + EPS)
    per = share // cols_e
    quarter = lax.dynamic_slice_in_dim(state_all, me_t * per, per, 1)
    state_q = jnp.transpose(quarter, (2, 1, 0, 3)).reshape(tok_count, share).astype(
        jnp.float32
    )
    gain_q = lax.dynamic_slice_in_dim(norm_gain, me_t * share, share, 0).astype(jnp.float32)
    normed_q = (state_q * scale * gain_q).astype(jnp.bfloat16)

    normed_q = with_layout_constraint(normed_q, Layout(major_to_minor=(0, 1)))
    slabs = lax.all_gather(normed_q, ("tensor", "expert"), axis=0, tiled=False)
    slabs = slabs.reshape(tensor_ways, all_tok, share)

    total = jnp.zeros((all_tok, share), jnp.float32)
    for loc in range(exp_local):
        gate = None
        upper = None
        for a in range(tensor_ways):
            x = slabs[a]
            gpart = jnp.dot(
                x, gate_proj[loc, :, a * share : (a + 1) * share].T,
                preferred_element_type=jnp.float32,
            )
            upart = jnp.dot(
                x, up_proj[loc, :, a * share : (a + 1) * share].T,
                preferred_element_type=jnp.float32,
            )
            gate = gpart if gate is None else gate + gpart
            upper = upart if upper is None else upper + upart
        act = (jax.nn.silu(gate) * upper).astype(jnp.bfloat16)
        act_all = lax.all_gather(act, "tensor", axis=1, tiled=True)
        out = jnp.dot(
            act_all, down_proj[loc], preferred_element_type=jnp.float32
        ).astype(jnp.bfloat16)
        w_tok = w_mine[:, loc][:, None]
        total = total + jnp.where(w_tok > 0, w_tok * out.astype(jnp.float32), 0.0)
    near = 2 if groups % 2 == 0 else 1
    far = groups // near
    pairs = [[z * near + x for x in range(near)] for z in range(far)]
    lines = [[z * near + x for z in range(far)] for x in range(near)]
    halves = lax.psum_scatter(
        total.astype(jnp.bfloat16).reshape(far, near * tok_count, share), "expert",
        scatter_dimension=0, tiled=True, axis_index_groups=lines,
    )
    mixture = lax.psum_scatter(
        halves.reshape(near * tok_count, share), "expert", scatter_dimension=0,
        tiled=True, axis_index_groups=pairs,
    )
    mixture = mixture.astype(jnp.float32)
    state_out = state_q
    return (state_out + mixture).astype(jnp.bfloat16)


def solution(mesh):
    in_specs = (
        P("expert", "tensor"),
        P("tensor", "expert"),
        P("expert", None),
        P(),
        P("expert", "tensor", None),
        P("expert", "tensor", None),
        P("expert", None, "tensor"),
        P("expert", None),
        P("expert", None),
    )
    out_specs = P("expert", "tensor")
    return jax.shard_map(
        on_device, mesh=mesh, in_specs=in_specs, out_specs=out_specs, check_vma=False
    )
```

```python
import jax
import jax.numpy as jnp
from jax import lax
from jax.sharding import PartitionSpec as P
from jax.experimental.layout import Layout, with_layout_constraint

EPS = 1e-06


def on_device(
    attn_heads,
    out_proj,
    residual,
    norm_gain,
    gate_proj,
    up_proj,
    down_proj,
    expert_ids,
    gate_scores,
):
    tok_count = residual.shape[0]
    width = residual.shape[1]
    groups = lax.axis_size("expert")
    tensor_ways = lax.axis_size("tensor")
    exp_local = gate_proj.shape[0]
    hidden_local = gate_proj.shape[1]
    share = width // tensor_ways
    cols_e = out_proj.shape[1]
    cols_et = cols_e // tensor_ways
    me_e = lax.axis_index("expert")
    me_t = lax.axis_index("tensor")
    all_tok = groups * tok_count

    experts_all = groups * exp_local
    hit_src = expert_ids[:, :, None] == jnp.arange(experts_all, dtype=jnp.int32)[None, None, :]
    weights = gate_scores / jnp.sum(gate_scores, axis=1, keepdims=True)
    w_src = jnp.sum(jnp.where(hit_src, weights[:, :, None], 0.0), axis=1)
    hi = w_src.astype(jnp.bfloat16)
    rest = w_src - hi.astype(jnp.float32)
    mid = rest.astype(jnp.bfloat16)
    lo = (rest - mid.astype(jnp.float32)).astype(jnp.bfloat16)
    coded = jnp.stack([hi, mid, lo]).reshape(-1)
    heads_w = attn_heads.shape[1]
    extra = -(-coded.shape[0] // (heads_w * 8)) * 8
    coded = jnp.pad(coded, (0, extra * heads_w - coded.shape[0])).reshape(extra, heads_w)
    packet = jnp.concatenate([attn_heads, coded], axis=0)

    got = lax.all_gather(packet, "expert", axis=0, tiled=False)
    partial = jnp.einsum(
        "enh,hc->enc", got[:, :tok_count], out_proj, preferred_element_type=jnp.float32
    ).reshape(all_tok, cols_e)
    parts = got[:, tok_count:].reshape(groups, -1)[:, : 3 * tok_count * experts_all]
    parts = parts.reshape(groups, 3, tok_count, experts_all).astype(jnp.float32)
    w_all = (parts[:, 0] + parts[:, 1] + parts[:, 2]).reshape(all_tok, experts_all)
    w_mine = lax.dynamic_slice_in_dim(w_all, me_e * exp_local, exp_local, 1)
    summed = lax.psum_scatter(partial, "tensor", scatter_dimension=1, tiled=True)
    res_out = lax.dynamic_index_in_dim(
        residual.reshape(tok_count, groups, tensor_ways, cols_et), me_t, 2, keepdims=False
    )
    res_in = lax.all_to_all(jnp.transpose(res_out, (1, 0, 2)), "expert", 0, 0, tiled=False)
    state_slab = (
        res_in.astype(jnp.float32) + summed.reshape(groups, tok_count, cols_et)
    ).astype(jnp.bfloat16)
    fan = jnp.broadcast_to(state_slab[:, None], (groups, tensor_ways) + state_slab.shape[1:])
    state_all = lax.all_to_all(
        fan.reshape((groups * tensor_ways,) + state_slab.shape[1:]),
        ("expert", "tensor"), 0, 0, tiled=False,
    ).reshape((groups, tensor_ways) + state_slab.shape[1:])
    state_sq = state_all.astype(jnp.float32)

    squares = jnp.sum(state_sq * state_sq, axis=(0, 1, 3))[:, None]
    scale = lax.rsqrt(squares / width + EPS)
    per = share // cols_e
    quarter = lax.dynamic_slice_in_dim(state_all, me_t * per, per, 0)
    state_q = jnp.transpose(quarter, (2, 0, 1, 3)).reshape(tok_count, share).astype(
        jnp.float32
    )
    gain_q = lax.dynamic_slice_in_dim(norm_gain, me_t * share, share, 0).astype(jnp.float32)
    normed_q = (state_q * scale * gain_q).astype(jnp.bfloat16)

    normed_q = with_layout_constraint(normed_q, Layout(major_to_minor=(0, 1)))
    slabs = lax.all_gather(normed_q, ("tensor", "expert"), axis=0, tiled=False)
    slabs = slabs.reshape(tensor_ways, all_tok, share)

    total = jnp.zeros((all_tok, share), jnp.float32)
    for loc in range(exp_local):
        gate = None
        upper = None
        for a in range(tensor_ways):
            x = slabs[a]
            gpart = jnp.dot(
                x, gate_proj[loc, :, a * share : (a + 1) * share].T,
                preferred_element_type=jnp.float32,
            )
            upart = jnp.dot(
                x, up_proj[loc, :, a * share : (a + 1) * share].T,
                preferred_element_type=jnp.float32,
            )
            gate = gpart if gate is None else gate + gpart
            upper = upart if upper is None else upper + upart
        act = (jax.nn.silu(gate) * upper).astype(jnp.bfloat16)
        act_all = lax.all_gather(act, "tensor", axis=1, tiled=True)
        out = jnp.dot(
            act_all, down_proj[loc], preferred_element_type=jnp.float32
        ).astype(jnp.bfloat16)
        w_tok = w_mine[:, loc][:, None]
        total = total + jnp.where(w_tok > 0, w_tok * out.astype(jnp.float32), 0.0)
    near = 2 if groups % 2 == 0 else 1
    far = groups // near
    pairs = [[z * near + x for x in range(near)] for z in range(far)]
    lines = [[z * near + x for z in range(far)] for x in range(near)]
    halves = lax.psum_scatter(
        total.astype(jnp.bfloat16).reshape(far, near * tok_count, share), "expert",
        scatter_dimension=0, tiled=True, axis_index_groups=lines,
    )
    mixture = lax.psum_scatter(
        halves.reshape(near * tok_count, share), "expert", scatter_dimension=0,
        tiled=True, axis_index_groups=pairs,
    )
    mixture = mixture.astype(jnp.float32)
    state_out = state_q
    return (state_out + mixture).astype(jnp.bfloat16)


def solution(mesh):
    in_specs = (
        P("expert", "tensor"),
        P("tensor", "expert"),
        P("expert", None),
        P(),
        P("expert", "tensor", None),
        P("expert", "tensor", None),
        P("expert", None, "tensor"),
        P("expert", None),
        P("expert", None),
    )
    out_specs = P("expert", "tensor")
    return jax.shard_map(
        on_device, mesh=mesh, in_specs=in_specs, out_specs=out_specs, check_vma=False
    )
```

```python
import jax
import jax.numpy as jnp
from jax import lax
from jax.sharding import PartitionSpec as P
from jax.experimental.layout import Layout, with_layout_constraint

EPS = 1e-06


def on_device(
    attn_heads,
    out_proj,
    residual,
    norm_gain,
    gate_proj,
    up_proj,
    down_proj,
    expert_ids,
    gate_scores,
):
    tok_count = residual.shape[0]
    width = residual.shape[1]
    groups = lax.axis_size("expert")
    tensor_ways = lax.axis_size("tensor")
    exp_local = gate_proj.shape[0]
    hidden_local = gate_proj.shape[1]
    share = width // tensor_ways
    cols_e = out_proj.shape[1]
    cols_et = cols_e // tensor_ways
    me_e = lax.axis_index("expert")
    me_t = lax.axis_index("tensor")
    all_tok = groups * tok_count

    experts_all = groups * exp_local
    hit_src = expert_ids[:, :, None] == jnp.arange(experts_all, dtype=jnp.int32)[None, None, :]
    weights = gate_scores / jnp.sum(gate_scores, axis=1, keepdims=True)
    w_src = jnp.sum(jnp.where(hit_src, weights[:, :, None], 0.0), axis=1)
    hi = w_src.astype(jnp.bfloat16)
    rest = w_src - hi.astype(jnp.float32)
    mid = rest.astype(jnp.bfloat16)
    lo = (rest - mid.astype(jnp.float32)).astype(jnp.bfloat16)
    coded = jnp.stack([hi, mid, lo]).reshape(-1)
    heads_w = attn_heads.shape[1]
    extra = -(-coded.shape[0] // (heads_w * 8)) * 8
    coded = jnp.pad(coded, (0, extra * heads_w - coded.shape[0])).reshape(extra, heads_w)
    packet = jnp.concatenate([attn_heads, coded], axis=0)

    got = lax.all_gather(packet, "expert", axis=0, tiled=False)
    partial = jnp.einsum(
        "enh,hc->enc", got[:, :tok_count], out_proj, preferred_element_type=jnp.float32
    ).reshape(all_tok, cols_e)
    parts = got[:, tok_count:].reshape(groups, -1)[:, : 3 * tok_count * experts_all]
    parts = parts.reshape(groups, 3, tok_count, experts_all).astype(jnp.float32)
    w_all = (parts[:, 0] + parts[:, 1] + parts[:, 2]).reshape(all_tok, experts_all)
    w_mine = lax.dynamic_slice_in_dim(w_all, me_e * exp_local, exp_local, 1)
    summed = lax.psum_scatter(partial, "tensor", scatter_dimension=1, tiled=True)
    res_out = lax.dynamic_index_in_dim(
        residual.reshape(tok_count, groups, tensor_ways, cols_et), me_t, 2, keepdims=False
    )
    res_in = lax.all_to_all(jnp.transpose(res_out, (1, 0, 2)), "expert", 0, 0, tiled=False)
    state_slab = (
        res_in.astype(jnp.float32) + summed.reshape(groups, tok_count, cols_et)
    ).astype(jnp.bfloat16)
    state_ct = lax.all_to_all(state_slab, "expert", 0, 0, tiled=False)
    state_all = lax.all_gather(state_ct, "tensor", axis=0, tiled=False)
    state_sq = state_all.astype(jnp.float32)

    squares = jnp.sum(state_sq * state_sq, axis=(0, 1, 3))[:, None]
    scale = lax.rsqrt(squares / width + EPS)
    per = share // cols_e
    quarter = lax.dynamic_slice_in_dim(state_all, me_t * per, per, 1)
    state_q = jnp.transpose(quarter, (2, 1, 0, 3)).reshape(tok_count, share).astype(
        jnp.float32
    )
    gain_q = lax.dynamic_slice_in_dim(norm_gain, me_t * share, share, 0).astype(jnp.float32)
    normed_q = (state_q * scale * gain_q).astype(jnp.bfloat16)

    normed_q = with_layout_constraint(normed_q, Layout(major_to_minor=(0, 1)))
    slabs = lax.all_gather(normed_q, ("tensor", "expert"), axis=0, tiled=False)
    slabs = slabs.reshape(tensor_ways, all_tok, share)

    total = jnp.zeros((all_tok, share), jnp.float32)
    for loc in range(exp_local):
        gate = None
        upper = None
        for a in range(tensor_ways):
            x = slabs[a]
            gpart = jnp.dot(
                x, gate_proj[loc, :, a * share : (a + 1) * share].T,
                preferred_element_type=jnp.float32,
            )
            upart = jnp.dot(
                x, up_proj[loc, :, a * share : (a + 1) * share].T,
                preferred_element_type=jnp.float32,
            )
            gate = gpart if gate is None else gate + gpart
            upper = upart if upper is None else upper + upart
        act = (jax.nn.silu(gate) * upper).astype(jnp.bfloat16)
        act_all = lax.all_gather(act, "tensor", axis=1, tiled=True)
        out = jnp.dot(
            act_all, down_proj[loc], preferred_element_type=jnp.float32
        ).astype(jnp.bfloat16)
        w_tok = w_mine[:, loc][:, None]
        total = total + w_tok * out.astype(jnp.float32)
    near = 2 if groups % 2 == 0 else 1
    far = groups // near
    pairs = [[z * near + x for x in range(near)] for z in range(far)]
    lines = [[z * near + x for z in range(far)] for x in range(near)]
    halves = lax.psum_scatter(
        total.astype(jnp.bfloat16).reshape(far, near * tok_count, share), "expert",
        scatter_dimension=0, tiled=True, axis_index_groups=lines,
    )
    mixture = lax.psum_scatter(
        halves.reshape(near * tok_count, share), "expert", scatter_dimension=0,
        tiled=True, axis_index_groups=pairs,
    )
    mixture = mixture.astype(jnp.float32)
    state_out = state_q
    return (state_out + mixture).astype(jnp.bfloat16)


def solution(mesh):
    in_specs = (
        P("expert", "tensor"),
        P("tensor", "expert"),
        P("expert", None),
        P(),
        P("expert", "tensor", None),
        P("expert", "tensor", None),
        P("expert", None, "tensor"),
        P("expert", None),
        P("expert", None),
    )
    out_specs = P("expert", "tensor")
    return jax.shard_map(
        on_device, mesh=mesh, in_specs=in_specs, out_specs=out_specs, check_vma=False
    )
```
